256 devices in a mesh: blk: 32 (over x, y, z_hi), head: 8 (over z_lo, core).
Axes of the slice: x: 4, y: 4, z: 8 (z_hi: 2, z_lo: 4; z = z_hi * 4 + z_lo), core: 2. Of those that a mesh axis runs over, the one named last changes fastest.
Arguments:
- tokens: bfloat16 [16384, 1408], P('blk'), may hold values from -6 to 6
- group_segment: int32 [4096], P('blk'), may hold values from 0 to 15, never falling along the last dimension, each value on 1 to 512 neighbouring positions
- ln1_gain: float32 [1408], replicated, may hold values from 0.1 to 1.9
- ln1_bias: float32 [1408], replicated, may hold values from -3 to 3
- qkv_weight: bfloat16 [1408, 3, 1408], P(None, None, 'head'), may hold values from -1 to 1
- out_weight: bfloat16 [1408, 1408], P('head'), may hold values from -0.15625 to 0.15625
- ln2_gain: float32 [1408], replicated, may hold values from 0.1 to 1.9
- ln2_bias: float32 [1408], replicated, may hold values from -3 to 3
- fc1_weight: bfloat16 [1408, 6144], P(None, 'head'), may hold values from -0.15625 to 0.15625
- fc2_weight: bfloat16 [6144, 1408], P('head'), may hold values from -0.078125 to 0.078125
- proj_weight: bfloat16 [5632, 4096], P('blk', 'head'), may hold values from -0.078125 to 0.078125
Outputs:
- merged_out: bfloat16 [4096, 4096], P('blk', 'head')
- req_rms: float32 [16], replicated
- req_peak: float32 [16], replicated
The draws below stay inside these ranges and needn't reach their ends.
Inputs may be any that keep to these rules, and one draw needn't show every extreme that they name: `group_segment`: ids never fall along the rows; every request holds 1 to 512 groups, and one holds exactly that many.
All inputs are finite; a program needn't handle non-finite values.
Results may differ from the reference program's by a relative error of at most 0.017.
Values may be sent and summed in bfloat16 or wider, within the bound.
No kernel may reach another device: no remote copies, remote signals or barrier semaphores. Data moves between devices by JAX's collectives and lax.ppermute only.
A program may use at most 64 MiB of HBM per device.

```python
import math
import jax
import jax.numpy as jnp
import numpy as np
from jax import lax

D = 1408
HEADS = 16
HD = 88
FF = 6144
OUTW = 4096
TOK_DEV = 512
REACH = 4
TOKENS = 16384
MERGED = 4096
SEGS = 16
N_BLK = 32
N_HEAD = 8


def draw_tokens(key, part):
    first = jax.random.fold_in(key, 0)
    base = jnp.clip(jax.random.normal(first, (TOKENS, D), jnp.float32), -6.0, 6.0)
    return base.astype(jnp.bfloat16)


def draw_qkv_weight(key, part):
    first = jax.random.fold_in(key, 0)
    base = jnp.clip(jax.random.normal(first, (D, 3, HEADS * HD), jnp.float32), -4.0, 4.0) * D ** (-0.5)
    return base.astype(jnp.bfloat16)


def shard_levels(rng, extent, cuts, low, largest):
    level = 1.0
    for dim, parts in cuts:
        heights = jax.random.uniform(jax.random.fold_in(jax.random.fold_in(rng, 6), dim), (parts,), jnp.float32, low / len(cuts), largest / len(cuts))
        level = level * jnp.repeat(jnp.exp(heights), extent[dim] // parts).reshape((-1,) + (1,) * (len(extent) - 1 - dim))
    return level


def split_up(count, total, bound, lean):
    loads = [(1 << 20) // math.isqrt(grade ** lean) + 1 for grade in range(2, count + 1)]
    rest, given = total - bound - (count - 1), [1] * (count - 1)
    while rest > 0:
        candidates = [i for i in range(count - 1) if given[i] < bound]
        pool, remaining = sum([loads[i] for i in candidates]), rest
        for i in candidates:
            more = min(bound - given[i], max(1, remaining * loads[i] // pool), rest)
            given[i] = given[i] + more
            rest = rest - more
    return np.array([bound] + given)


def ragged(own_key, number_of, total, reach, slope):
    if number_of == 2:
        one = jax.random.randint(own_key, (), max(1, total - reach), min(reach, total - 1) + 1)
        return jnp.stack([one, total - one])
    tallies = jnp.asarray(split_up(number_of, total, reach, slope), jnp.int32)
    twos = (number_of - 1) // 2
    giver, taker = tallies[1:1 + 2 * twos:2], tallies[2:2 + 2 * twos:2]
    margin = jnp.minimum(giver - 1, reach - taker)
    passed = jax.random.randint(jax.random.fold_in(own_key, 1), (twos,), 0, 1 << 20) % (margin + 1)
    tallies = tallies.at[1:1 + 2 * twos:2].set(giver - passed).at[2:2 + 2 * twos:2].set(taker + passed)
    return tallies[jax.random.permutation(jax.random.fold_in(own_key, 2), number_of)]


def bell_draw(stream_key, dims, scale, bound, pieces=(), held_as=jnp.bfloat16):
    level = shard_levels(stream_key, dims, pieces, -0.22, 0.18) if pieces else 1.0
    result = jax.random.normal(stream_key, dims, jnp.float32) * scale * level
    return jnp.minimum(jnp.maximum(result, -bound), bound).astype(held_as)


def setup_inputs(seed: int = 0) -> dict:
    key_of = jax.random.split(jax.random.key(seed), 12)
    return {
        "tokens": draw_tokens(jax.random.fold_in(key_of[11], 71), 0),
        "group_segment": jnp.searchsorted(jnp.cumsum(ragged(key_of[1], SEGS, MERGED, REACH * TOK_DEV // 4, 2)), jnp.arange(MERGED), side="right").astype(jnp.int32),
        "ln1_gain": jnp.clip(1.0 + 0.18 * jax.random.normal(key_of[2], (D,), jnp.float32), 0.1, 1.9),
        "ln1_bias": bell_draw(key_of[3], (D,), 0.5, 3.0, (), jnp.float32),
        "qkv_weight": draw_qkv_weight(jax.random.fold_in(key_of[11], 71), 0),
        "out_weight": bell_draw(key_of[5], (HEADS * HD, D), (HEADS * HD) ** -0.5, 0.15625, ((0, 8),)),
        "ln2_gain": jnp.clip(1.0 + 0.18 * jax.random.normal(key_of[6], (D,), jnp.float32), 0.1, 1.9),
        "ln2_bias": bell_draw(key_of[7], (D,), 0.5, 3.0, (), jnp.float32),
        "fc1_weight": bell_draw(key_of[8], (D, FF), D ** -0.5, 0.15625, ((1, 8),)),
        "fc2_weight": bell_draw(key_of[9], (FF, D), FF ** -0.5, 0.078125, ((0, 8),)),
        "proj_weight": bell_draw(key_of[10], (4 * D, OUTW), (4 * D) ** -0.5, 0.078125, ((0, 32), (1, 8))),
    }


def layer_norm(x, gain, bias):
    mean = lax.optimization_barrier(jnp.mean(x, axis=-1, keepdims=True))
    var = lax.optimization_barrier(jnp.mean((x - mean) ** 2, axis=-1, keepdims=True))
    return (x - mean) * lax.rsqrt(var + 1e-06) * gain + bias

def reference(tokens, group_segment, ln1_gain, ln1_bias, qkv_weight, out_weight, ln2_gain, ln2_bias, fc1_weight, fc2_weight, proj_weight):
    x_in = tokens.astype(jnp.float32)
    seg = jnp.repeat(group_segment, 4).astype(jnp.int32)
    normed = layer_norm(x_in, ln1_gain, ln1_bias).astype(jnp.bfloat16)
    qkv = jnp.einsum('rd,dck->crk', normed.astype(jnp.float32), qkv_weight.astype(jnp.float32)).astype(jnp.bfloat16)
    query = qkv[0].reshape(TOKENS, HEADS, HD)
    keys = qkv[1].reshape(TOKENS, HEADS, HD)
    values = qkv[2].reshape(TOKENS, HEADS, HD)
    wide = REACH * TOK_DEV
    keys_pad = jnp.pad(keys, ((wide, wide), (0, 0), (0, 0)))
    values_pad = jnp.pad(values, ((wide, wide), (0, 0), (0, 0)))
    seg_pad = jnp.pad(seg, (wide, wide), constant_values=-1)
    span = TOK_DEV + 2 * wide
    scale = 1.0 / HD ** 0.5

    def one_block(index):
        start = (index * TOK_DEV).astype(jnp.int32)
        qblock = lax.dynamic_slice_in_dim(query, start, TOK_DEV, 0).astype(jnp.float32)
        qseg = lax.dynamic_slice_in_dim(seg, start, TOK_DEV, 0)
        kblock = lax.dynamic_slice_in_dim(keys_pad, start, span, 0).astype(jnp.float32)
        vblock = lax.dynamic_slice_in_dim(values_pad, start, span, 0).astype(jnp.float32)
        kseg = lax.dynamic_slice_in_dim(seg_pad, start, span, 0)
        scores = jnp.einsum('rhe,phe->hrp', qblock, kblock) * scale
        mask = (qseg[:, None] == kseg[None, :])[None]
        top = lax.optimization_barrier(jnp.max(jnp.where(mask, scores, -1e+30), axis=-1, keepdims=True))
        weights = jnp.where(mask, jnp.exp(scores - top), 0.0)
        total = lax.optimization_barrier(jnp.sum(weights, axis=-1))
        rounded = weights.astype(jnp.bfloat16).astype(jnp.float32)
        summed = jnp.einsum('hrp,phe->rhe', rounded, vblock)
        out = summed / jnp.transpose(total)[:, :, None]
        return out.astype(jnp.bfloat16).reshape(TOK_DEV, HEADS * HD)
    attn = lax.map(one_block, jnp.arange(N_BLK, dtype=jnp.int32)).reshape(TOKENS, HEADS * HD)
    cols = HEADS * HD // N_HEAD
    attn_total = jnp.zeros((TOKENS, D), jnp.float32)
    for group in range(N_HEAD):
        part = jnp.dot(attn[:, group * cols:(group + 1) * cols], out_weight[group * cols:(group + 1) * cols], preferred_element_type=jnp.float32)
        attn_total = attn_total + part.astype(jnp.bfloat16).astype(jnp.float32)
    h_one = x_in + attn_total
    n_two = layer_norm(h_one, ln2_gain, ln2_bias).astype(jnp.bfloat16)
    hidden = jax.nn.gelu(jnp.dot(n_two, fc1_weight, preferred_element_type=jnp.float32), approximate=False).astype(jnp.bfloat16)
    units = FF // N_HEAD
    mlp_total = jnp.zeros((TOKENS, D), jnp.float32)
    for group in range(N_HEAD):
        part = jnp.dot(hidden[:, group * units:(group + 1) * units], fc2_weight[group * units:(group + 1) * units], preferred_element_type=jnp.float32)
        mlp_total = mlp_total + part.astype(jnp.bfloat16).astype(jnp.float32)
    layer = (h_one + mlp_total).astype(jnp.bfloat16)
    grouped = layer.reshape(MERGED, 4 * D)
    proj = jnp.dot(grouped, proj_weight, preferred_element_type=jnp.float32)
    row_sq = lax.optimization_barrier(jnp.sum(proj * proj, axis=1))
    onehot = group_segment[:, None] == jnp.arange(SEGS, dtype=jnp.int32)[None, :]
    tot_sq = lax.optimization_barrier(jnp.sum(jnp.where(onehot, row_sq[:, None], 0.0), axis=0))
    counts = lax.optimization_barrier(jnp.sum(jnp.where(onehot, 1.0, 0.0), axis=0)).astype(jnp.float32)
    req_rms = jnp.sqrt(tot_sq / (counts * OUTW) + 1e-06)
    row_top = lax.optimization_barrier(jnp.max(jnp.abs(proj), axis=1))
    req_peak = lax.optimization_barrier(jnp.max(jnp.where(onehot, row_top[:, None], 0.0), axis=0))
    merged_out = (proj / req_rms[group_segment][:, None]).astype(jnp.bfloat16)
    return (merged_out, req_rms, req_peak)
```

```python
import jax
import jax.numpy as jnp
from jax import lax
from jax.sharding import PartitionSpec as P

HD = 88
OUTW = 4096
REACH = 4


def passed_along(x, axis, by):
    size = lax.axis_size(axis)
    pairs = [(i, i + by) for i in range(size) if 0 <= i + by < size]
    return lax.ppermute(x, axis, pairs)


def butterfly(summed, peak):
    split = summed.shape[0]
    both = jnp.concatenate([summed, peak])
    for axis in ("head", "blk"):
        size = lax.axis_size(axis)
        if size & (size - 1):
            both = jnp.concatenate(
                [lax.psum(both[:split], axis), lax.pmax(both[split:], axis)]
            )
            continue
        step = 1
        while step < size:
            pairs = [(i, i ^ step) for i in range(size)]
            other = lax.ppermute(both, axis, pairs)
            both = jnp.concatenate(
                [both[:split] + other[:split], jnp.maximum(both[split:], other[split:])]
            )
            step *= 2
    return both[:split], both[split:]


def layer_norm(x, gain, bias):
    mean = jnp.mean(x, axis=-1, keepdims=True)
    var = jnp.mean((x - mean) ** 2, axis=-1, keepdims=True)
    return (x - mean) * lax.rsqrt(var + 1e-06) * gain + bias


def per_device(
    tokens,
    group_segment,
    ln1_gain,
    ln1_bias,
    qkv_weight,
    out_weight,
    ln2_gain,
    ln2_bias,
    fc1_weight,
    fc2_weight,
    proj_weight,
):
    rows = tokens.shape[0]
    x_in = tokens.astype(jnp.float32)
    seg_ids = jnp.repeat(group_segment + 1, 4)
    own_low = jnp.min(seg_ids)
    own_high = jnp.max(seg_ids)
    normed = layer_norm(x_in, ln1_gain, ln1_bias).astype(jnp.bfloat16)
    qkv = jnp.einsum("rd,dck->crk", normed, qkv_weight, preferred_element_type=jnp.float32).astype(
        jnp.bfloat16
    )
    local_heads = qkv.shape[2] // HD
    query = qkv[0].reshape(rows, local_heads, HD)
    keys = qkv[1]
    values = qkv[2]
    scale = 1.0 / HD**0.5

    def update(carry, piece):
        top, total, acc = carry
        kpiece, vpiece, ipiece = piece
        count = kpiece.shape[0]
        scores = (
            jnp.einsum(
                "rhe,phe->hrp",
                query,
                kpiece.reshape(count, local_heads, HD),
                preferred_element_type=jnp.float32,
            )
            * scale
        )
        mask = (seg_ids[:, None] == ipiece[None, :])[None]
        new_top = jnp.maximum(top, jnp.max(jnp.where(mask, scores, -1e30), axis=-1))
        factor = jnp.exp(top - new_top)
        weights = jnp.where(mask, jnp.exp(scores - new_top[..., None]), 0.0)
        total = total * factor + jnp.sum(weights, axis=-1)
        acc = acc * factor[..., None] + jnp.einsum(
            "hrp,phe->hre",
            weights.astype(jnp.bfloat16),
            vpiece.reshape(count, local_heads, HD),
            preferred_element_type=jnp.float32,
        )
        return (new_top, total, acc)

    def fold_block(carry, piece):
        ipiece = piece[2]
        touches = (jnp.min(ipiece) <= own_high) & (jnp.max(ipiece) >= own_low)
        return lax.cond(touches, lambda c: update(c, piece), lambda c: c, carry)

    start_state = (
        jnp.full((local_heads, rows), -1e30, jnp.float32),
        jnp.zeros((local_heads, rows), jnp.float32),
        jnp.zeros((local_heads, rows, HD), jnp.float32),
    )
    state = fold_block(start_state, (keys, values, seg_ids))
    width = keys.shape[1]
    packed = jnp.concatenate(
        [keys, values, seg_ids.astype(jnp.bfloat16)[:, None]], axis=1
    )
    packed = jnp.pad(packed, ((0, 0), (0, (-packed.shape[1]) % 128)))
    for distance in range(1, REACH + 1):
        for offset in (distance, -distance):
            got = passed_along(packed, "blk", offset)
            piece = (
                got[:, :width],
                got[:, width : 2 * width],
                got[:, 2 * width].astype(jnp.int32),
            )
            state = fold_block(state, piece)
    top, total, acc = state
    attn = (acc / total[..., None]).astype(jnp.bfloat16)
    attn = jnp.transpose(attn, (1, 0, 2)).reshape(rows, local_heads * HD)
    attn_part = jnp.dot(attn, out_weight, preferred_element_type=jnp.float32)
    h_one = x_in + lax.psum(attn_part.astype(jnp.bfloat16), "head").astype(jnp.float32)
    n_two = layer_norm(h_one, ln2_gain, ln2_bias).astype(jnp.bfloat16)
    hidden = jax.nn.gelu(
        jnp.dot(n_two, fc1_weight, preferred_element_type=jnp.float32), approximate=False
    ).astype(jnp.bfloat16)
    mlp_part = jnp.dot(hidden, fc2_weight, preferred_element_type=jnp.float32)
    layer = (h_one + lax.psum(mlp_part.astype(jnp.bfloat16), "head").astype(jnp.float32)).astype(
        jnp.bfloat16
    )
    grouped = layer.reshape(rows // 4, 4 * layer.shape[1])
    proj = jnp.dot(
        grouped,
        lax.all_gather(proj_weight, "blk", axis=0, tiled=True),
        preferred_element_type=jnp.float32,
    )
    requests = lax.axis_size("blk") // 2
    onehot = (group_segment[:, None] == jnp.arange(requests, dtype=jnp.int32)[None, :]).astype(
        jnp.float32
    )
    row_sq = jnp.sum(proj * proj, axis=1)
    local_sq = jnp.dot(row_sq, onehot, precision=lax.Precision.HIGHEST)
    local_count = jnp.sum(onehot, axis=0)
    row_top = jnp.max(jnp.abs(proj), axis=1)
    local_peak = jnp.max(jnp.where(onehot > 0.0, row_top[:, None], 0.0), axis=0)
    summed, req_peak = butterfly(jnp.concatenate([local_sq, local_count]), local_peak)
    tot_sq, tot_count = summed[:requests], summed[requests:]
    counts = tot_count / lax.axis_size("head")
    req_rms = jnp.sqrt(tot_sq / (counts * OUTW) + 1e-06)
    row_rms = jnp.dot(onehot, req_rms, precision=lax.Precision.HIGHEST)
    merged_out = (proj / row_rms[:, None]).astype(jnp.bfloat16)
    return (merged_out, req_rms, req_peak)


def solution(mesh):
    placed = (
        P("blk", None),
        P("blk"),
        P(),
        P(),
        P(None, None, "head"),
        P("head", None),
        P(),
        P(),
        P(None, "head"),
        P("head", None),
        P("blk", "head"),
    )
    return jax.shard_map(
        per_device,
        mesh=mesh,
        in_specs=placed,
        out_specs=(P("blk", "head"), P(), P()),
        check_vma=False,
    )
```

```python
import jax
import jax.numpy as jnp
from jax import lax
from jax.sharding import PartitionSpec as P

HD = 88
OUTW = 4096
REACH = 4


def passed_along(x, axis, by):
    size = lax.axis_size(axis)
    pairs = [(i, i + by) for i in range(size) if 0 <= i + by < size]
    return lax.ppermute(x, axis, pairs)


def butterfly(summed, peak):
    split = summed.shape[0]
    both = jnp.concatenate([summed, peak])
    for axis in ("head", "blk"):
        size = lax.axis_size(axis)
        if size & (size - 1):
            both = jnp.concatenate(
                [lax.psum(both[:split], axis), lax.pmax(both[split:], axis)]
            )
            continue
        step = 1
        while step < size:
            pairs = [(i, i ^ step) for i in range(size)]
            other = lax.ppermute(both, axis, pairs)
            both = jnp.concatenate(
                [both[:split] + other[:split], jnp.maximum(both[split:], other[split:])]
            )
            step *= 2
    return both[:split], both[split:]


def gather_rows(x, n_head):
    spread = jnp.broadcast_to(x[None], (n_head,) + x.shape)
    got = lax.all_to_all(spread, "head", 0, 0, tiled=True)
    return got.reshape((n_head * x.shape[0],) + x.shape[1:])


def layer_norm(x, gain, bias):
    mean = jnp.mean(x, axis=-1, keepdims=True)
    var = jnp.mean((x - mean) ** 2, axis=-1, keepdims=True)
    return (x - mean) * lax.rsqrt(var + 1e-06) * gain + bias


def per_device(
    tokens,
    group_segment,
    ln1_gain,
    ln1_bias,
    qkv_weight,
    out_weight,
    ln2_gain,
    ln2_bias,
    fc1_weight,
    fc2_weight,
    proj_weight,
):
    rows = tokens.shape[0]
    x_in = tokens.astype(jnp.float32)
    seg_ids = jnp.repeat(group_segment + 1, 4)
    own_low = jnp.min(seg_ids)
    own_high = jnp.max(seg_ids)
    normed = layer_norm(x_in, ln1_gain, ln1_bias).astype(jnp.bfloat16)
    qkv = jnp.einsum("rd,dck->crk", normed, qkv_weight, preferred_element_type=jnp.float32).astype(
        jnp.bfloat16
    )
    local_heads = qkv.shape[2] // HD
    query = qkv[0].reshape(rows, local_heads, HD)
    keys = qkv[1]
    values = qkv[2]
    scale = 1.0 / HD**0.5

    def update(carry, piece):
        top, total, acc = carry
        kpiece, vpiece, ipiece = piece
        count = kpiece.shape[0]
        scores = (
            jnp.einsum(
                "rhe,phe->hrp",
                query,
                kpiece.reshape(count, local_heads, HD),
                preferred_element_type=jnp.float32,
            )
            * scale
        )
        mask = (seg_ids[:, None] == ipiece[None, :])[None]
        new_top = jnp.maximum(top, jnp.max(jnp.where(mask, scores, -1e30), axis=-1))
        factor = jnp.exp(top - new_top)
        weights = jnp.where(mask, jnp.exp(scores - new_top[..., None]), 0.0)
        total = total * factor + jnp.sum(weights, axis=-1)
        acc = acc * factor[..., None] + jnp.einsum(
            "hrp,phe->hre",
            weights.astype(jnp.bfloat16),
            vpiece.reshape(count, local_heads, HD),
            preferred_element_type=jnp.float32,
        )
        return (new_top, total, acc)

    def fold_block(carry, piece):
        ipiece = piece[2]
        touches = (jnp.min(ipiece) <= own_high) & (jnp.max(ipiece) >= own_low)
        return lax.cond(touches, lambda c: update(c, piece), lambda c: c, carry)

    start_state = (
        jnp.full((local_heads, rows), -1e30, jnp.float32),
        jnp.zeros((local_heads, rows), jnp.float32),
        jnp.zeros((local_heads, rows, HD), jnp.float32),
    )
    state = fold_block(start_state, (keys, values, seg_ids))
    width = keys.shape[1]
    packed = jnp.concatenate(
        [keys, values, seg_ids.astype(jnp.bfloat16)[:, None]], axis=1
    )
    packed = jnp.pad(packed, ((0, 0), (0, (-packed.shape[1]) % 128)))
    for distance in range(1, REACH + 1):
        for offset in (distance, -distance):
            got = passed_along(packed, "blk", offset)
            piece = (
                got[:, :width],
                got[:, width : 2 * width],
                got[:, 2 * width].astype(jnp.int32),
            )
            state = fold_block(state, piece)
    top, total, acc = state
    attn = (acc / total[..., None]).astype(jnp.bfloat16)
    attn = jnp.transpose(attn, (1, 0, 2)).reshape(rows, local_heads * HD)
    n_head = lax.axis_size("head")
    share = rows // n_head
    width = x_in.shape[1]
    attn_rows = lax.all_to_all(attn, "head", 0, 1, tiled=True)
    full_out_weight = lax.all_gather(out_weight, "head", axis=0, tiled=True)
    x_mine = lax.dynamic_slice_in_dim(x_in, lax.axis_index("head") * share, share, 0)
    h_one = x_mine + jnp.dot(attn_rows, full_out_weight, preferred_element_type=jnp.float32)
    n_two = gather_rows(layer_norm(h_one, ln2_gain, ln2_bias).astype(jnp.bfloat16), n_head)
    hidden = jax.nn.gelu(
        jnp.dot(n_two, fc1_weight, preferred_element_type=jnp.float32), approximate=False
    ).astype(jnp.bfloat16)
    mlp_part = jnp.dot(hidden, fc2_weight, preferred_element_type=jnp.float32).astype(jnp.bfloat16)
    pieces = lax.all_to_all(mlp_part.reshape(n_head, share, width), "head", 0, 0, tiled=True)
    layer = gather_rows(
        (h_one + jnp.sum(pieces.astype(jnp.float32), axis=0)).astype(jnp.bfloat16), n_head
    )
    grouped = layer.reshape(rows // 4, 4 * layer.shape[1])
    proj = jnp.dot(
        grouped,
        lax.all_gather(proj_weight, "blk", axis=0, tiled=True),
        preferred_element_type=jnp.float32,
    )
    requests = lax.axis_size("blk") // 2
    onehot = (group_segment[:, None] == jnp.arange(requests, dtype=jnp.int32)[None, :]).astype(
        jnp.float32
    )
    row_sq = jnp.sum(proj * proj, axis=1)
    local_sq = jnp.dot(row_sq, onehot, precision=lax.Precision.HIGHEST)
    local_count = jnp.sum(onehot, axis=0)
    row_top = jnp.max(jnp.abs(proj), axis=1)
    local_peak = jnp.max(jnp.where(onehot > 0.0, row_top[:, None], 0.0), axis=0)
    summed, req_peak = butterfly(jnp.concatenate([local_sq, local_count]), local_peak)
    tot_sq, tot_count = summed[:requests], summed[requests:]
    counts = tot_count / lax.axis_size("head")
    req_rms = jnp.sqrt(tot_sq / (counts * OUTW) + 1e-06)
    row_rms = jnp.dot(onehot, req_rms, precision=lax.Precision.HIGHEST)
    merged_out = (proj / row_rms[:, None]).astype(jnp.bfloat16)
    return (merged_out, req_rms, req_peak)


def solution(mesh):
    placed = (
        P("blk", None),
        P("blk"),
        P(),
        P(),
        P(None, None, "head"),
        P("head", None),
        P(),
        P(),
        P(None, "head"),
        P("head", None),
        P("blk", "head"),
    )
    return jax.shard_map(
        per_device,
        mesh=mesh,
        in_specs=placed,
        out_specs=(P("blk", "head"), P(), P()),
        check_vma=False,
    )
```

```python
import jax
import jax.numpy as jnp
from jax import lax
from jax.sharding import PartitionSpec as P

HD = 88
OUTW = 4096
REACH = 4


def passed_along(x, axis, by):
    size = lax.axis_size(axis)
    pairs = [(i, i + by) for i in range(size) if 0 <= i + by < size]
    return lax.ppermute(x, axis, pairs)


def butterfly(summed, peak):
    split = summed.shape[0]
    both = jnp.concatenate([summed, peak])
    for axis in ("head", "blk"):
        size = lax.axis_size(axis)
        if size & (size - 1):
            both = jnp.concatenate(
                [lax.psum(both[:split], axis), lax.pmax(both[split:], axis)]
            )
            continue
        step = 1
        while step < size:
            pairs = [(i, i ^ step) for i in range(size)]
            other = lax.ppermute(both, axis, pairs)
            both = jnp.concatenate(
                [both[:split] + other[:split], jnp.maximum(both[split:], other[split:])]
            )
            step *= 2
    return both[:split], both[split:]


def gather_rows(x, n_head):
    spread = jnp.broadcast_to(x[None], (n_head,) + x.shape)
    got = lax.all_to_all(spread, "head", 0, 0, tiled=True)
    return got.reshape((n_head * x.shape[0],) + x.shape[1:])


def layer_norm(x, gain, bias):
    mean = jnp.mean(x, axis=-1, keepdims=True)
    var = jnp.mean((x - mean) ** 2, axis=-1, keepdims=True)
    return (x - mean) * lax.rsqrt(var + 1e-06) * gain + bias


def per_device(
    tokens,
    group_segment,
    ln1_gain,
    ln1_bias,
    qkv_weight,
    out_weight,
    ln2_gain,
    ln2_bias,
    fc1_weight,
    fc2_weight,
    proj_weight,
):
    rows = tokens.shape[0]
    x_in = tokens.astype(jnp.float32)
    seg_ids = jnp.repeat(group_segment + 1, 4)
    own_low = jnp.min(seg_ids)
    own_high = jnp.max(seg_ids)
    normed = layer_norm(x_in, ln1_gain, ln1_bias).astype(jnp.bfloat16)
    qkv = jnp.einsum("rd,dck->crk", normed, qkv_weight, preferred_element_type=jnp.float32).astype(
        jnp.bfloat16
    )
    local_heads = qkv.shape[2] // HD
    query = qkv[0].reshape(rows, local_heads, HD)
    keys = qkv[1]
    values = qkv[2]
    scale = 1.0 / HD**0.5

    def update(carry, piece):
        top, total, acc = carry
        kpiece, vpiece, ipiece = piece
        count = kpiece.shape[0]
        scores = (
            jnp.einsum(
                "rhe,phe->hrp",
                query,
                kpiece.reshape(count, local_heads, HD),
                preferred_element_type=jnp.float32,
            )
            * scale
        )
        mask = (seg_ids[:, None] == ipiece[None, :])[None]
        new_top = jnp.maximum(top, jnp.max(jnp.where(mask, scores, -1e30), axis=-1))
        factor = jnp.exp(top - new_top)
        weights = jnp.where(mask, jnp.exp(scores - new_top[..., None]), 0.0)
        total = total * factor + jnp.sum(weights, axis=-1)
        acc = acc * factor[..., None] + jnp.einsum(
            "hrp,phe->hre",
            weights.astype(jnp.bfloat16),
            vpiece.reshape(count, local_heads, HD),
            preferred_element_type=jnp.float32,
        )
        return (new_top, total, acc)

    def fold_block(carry, piece):
        ipiece = piece[2]
        touches = (jnp.min(ipiece) <= own_high) & (jnp.max(ipiece) >= own_low)
        return lax.cond(touches, lambda c: update(c, piece), lambda c: c, carry)

    start_state = (
        jnp.full((local_heads, rows), -1e30, jnp.float32),
        jnp.zeros((local_heads, rows), jnp.float32),
        jnp.zeros((local_heads, rows, HD), jnp.float32),
    )
    state = fold_block(start_state, (keys, values, seg_ids))
    width = keys.shape[1]
    packed = jnp.concatenate(
        [keys, values, seg_ids.astype(jnp.bfloat16)[:, None]], axis=1
    )
    packed = jnp.pad(packed, ((0, 0), (0, (-packed.shape[1]) % 128)))
    for distance in range(1, REACH + 1):
        for offset in (distance, -distance):
            got = passed_along(packed, "blk", offset)
            piece = (
                got[:, :width],
                got[:, width : 2 * width],
                got[:, 2 * width].astype(jnp.int32),
            )
            state = fold_block(state, piece)
    top, total, acc = state
    attn = (acc / total[..., None]).astype(jnp.bfloat16)
    attn = jnp.transpose(attn, (1, 0, 2)).reshape(rows, local_heads * HD)
    n_head = lax.axis_size("head")
    share = rows // n_head
    width = x_in.shape[1]
    full_proj_weight = lax.all_gather(proj_weight, "blk", axis=0, tiled=True)
    attn, full_proj_weight = lax.optimization_barrier((attn, full_proj_weight))
    attn_rows = lax.all_to_all(attn, "head", 0, 1, tiled=True)
    full_out_weight = lax.all_gather(out_weight, "head", axis=0, tiled=True)
    x_mine = lax.dynamic_slice_in_dim(x_in, lax.axis_index("head") * share, share, 0)
    h_one = x_mine + jnp.dot(attn_rows, full_out_weight, preferred_element_type=jnp.float32)
    n_two = gather_rows(layer_norm(h_one, ln2_gain, ln2_bias).astype(jnp.bfloat16), n_head)
    hidden = jax.nn.gelu(
        jnp.dot(n_two, fc1_weight, preferred_element_type=jnp.float32), approximate=False
    ).astype(jnp.bfloat16)
    mlp_part = jnp.dot(hidden, fc2_weight, preferred_element_type=jnp.float32).astype(jnp.bfloat16)
    pieces = lax.all_to_all(mlp_part.reshape(n_head, share, width), "head", 0, 0, tiled=True)
    layer = gather_rows(
        (h_one + jnp.sum(pieces.astype(jnp.float32), axis=0)).astype(jnp.bfloat16), n_head
    )
    grouped = layer.reshape(rows // 4, 4 * layer.shape[1])
    proj = jnp.dot(
        grouped,
        full_proj_weight,
        preferred_element_type=jnp.float32,
    )
    requests = lax.axis_size("blk") // 2
    onehot = (group_segment[:, None] == jnp.arange(requests, dtype=jnp.int32)[None, :]).astype(
        jnp.float32
    )
    row_sq = jnp.sum(proj * proj, axis=1)
    local_sq = jnp.dot(row_sq, onehot, precision=lax.Precision.HIGHEST)
    local_count = jnp.sum(onehot, axis=0)
    row_top = jnp.max(jnp.abs(proj), axis=1)
    local_peak = jnp.max(jnp.where(onehot > 0.0, row_top[:, None], 0.0), axis=0)
    summed, req_peak = butterfly(jnp.concatenate([local_sq, local_count]), local_peak)
    tot_sq, tot_count = summed[:requests], summed[requests:]
    counts = tot_count / lax.axis_size("head")
    req_rms = jnp.sqrt(tot_sq / (counts * OUTW) + 1e-06)
    row_rms = jnp.dot(onehot, req_rms, precision=lax.Precision.HIGHEST)
    merged_out = (proj / row_rms[:, None]).astype(jnp.bfloat16)
    return (merged_out, req_rms, req_peak)


def solution(mesh):
    placed = (
        P("blk", None),
        P("blk"),
        P(),
        P(),
        P(None, None, "head"),
        P("head", None),
        P(),
        P(),
        P(None, "head"),
        P("head", None),
        P("blk", "head"),
    )
    return jax.shard_map(
        per_device,
        mesh=mesh,
        in_specs=placed,
        out_specs=(P("blk", "head"), P(), P()),
        check_vma=False,
    )
```

```python
import jax
import jax.numpy as jnp
from jax import lax
from jax.sharding import PartitionSpec as P

HD = 88
OUTW = 4096
REACH = 4


def passed_along(x, axis, by):
    size = lax.axis_size(axis)
    pairs = [(i, i + by) for i in range(size) if 0 <= i + by < size]
    return lax.ppermute(x, axis, pairs)


def butterfly(summed, peak):
    split = summed.shape[0]
    both = jnp.concatenate([summed, peak])
    for axis in ("head", "blk"):
        size = lax.axis_size(axis)
        if size & (size - 1):
            both = jnp.concatenate(
                [lax.psum(both[:split], axis), lax.pmax(both[split:], axis)]
            )
            continue
        step = 1
        while step < size:
            pairs = [(i, i ^ step) for i in range(size)]
            other = lax.ppermute(both, axis, pairs)
            both = jnp.concatenate(
                [both[:split] + other[:split], jnp.maximum(both[split:], other[split:])]
            )
            step *= 2
    return both[:split], both[split:]


def gather_rows(x, n_head):
    spread = jnp.broadcast_to(x[None], (n_head,) + x.shape)
    got = lax.all_to_all(spread, "head", 0, 0, tiled=True)
    return got.reshape((n_head * x.shape[0],) + x.shape[1:])


def layer_norm(x, gain, bias):
    mean = jnp.mean(x, axis=-1, keepdims=True)
    var = jnp.mean((x - mean) ** 2, axis=-1, keepdims=True)
    return (x - mean) * lax.rsqrt(var + 1e-06) * gain + bias


def per_device(
    tokens,
    group_segment,
    ln1_gain,
    ln1_bias,
    qkv_weight,
    out_weight,
    ln2_gain,
    ln2_bias,
    fc1_weight,
    fc2_weight,
    proj_weight,
):
    rows = tokens.shape[0]
    x_in = tokens.astype(jnp.float32)
    seg_ids = jnp.repeat(group_segment + 1, 4)
    own_low = jnp.min(seg_ids)
    own_high = jnp.max(seg_ids)
    normed = layer_norm(x_in, ln1_gain, ln1_bias).astype(jnp.bfloat16)
    qkv = jnp.einsum("rd,dck->crk", normed, qkv_weight, preferred_element_type=jnp.float32).astype(
        jnp.bfloat16
    )
    local_heads = qkv.shape[2] // HD
    query = qkv[0].reshape(rows, local_heads, HD)
    keys = qkv[1]
    values = qkv[2]
    scale = 1.0 / HD**0.5

    def update(carry, piece):
        top, total, acc = carry
        kpiece, vpiece, ipiece = piece
        count = kpiece.shape[0]
        scores = (
            jnp.einsum(
                "rhe,phe->hrp",
                query,
                kpiece.reshape(count, local_heads, HD),
                preferred_element_type=jnp.float32,
            )
            * scale
        )
        mask = (seg_ids[:, None] == ipiece[None, :])[None]
        new_top = jnp.maximum(top, jnp.max(jnp.where(mask, scores, -1e30), axis=-1))
        factor = jnp.exp(top - new_top)
        weights = jnp.where(mask, jnp.exp(scores - new_top[..., None]), 0.0)
        total = total * factor + jnp.sum(weights, axis=-1)
        acc = acc * factor[..., None] + jnp.einsum(
            "hrp,phe->hre",
            weights.astype(jnp.bfloat16),
            vpiece.reshape(count, local_heads, HD),
            preferred_element_type=jnp.float32,
        )
        return (new_top, total, acc)

    def fold_block(carry, piece):
        ipiece = piece[2]
        touches = (jnp.min(ipiece) <= own_high) & (jnp.max(ipiece) >= own_low)
        return lax.cond(touches, lambda c: update(c, piece), lambda c: c, carry)

    start_state = (
        jnp.full((local_heads, rows), -1e30, jnp.float32),
        jnp.zeros((local_heads, rows), jnp.float32),
        jnp.zeros((local_heads, rows, HD), jnp.float32),
    )
    state = fold_block(start_state, (keys, values, seg_ids))
    width = keys.shape[1]
    packed = jnp.concatenate(
        [keys, values, seg_ids.astype(jnp.bfloat16)[:, None]], axis=1
    )
    packed = jnp.pad(packed, ((0, 0), (0, (-packed.shape[1]) % 128)))
    for distance in range(1, REACH + 1):
        for offset in (distance, -distance):
            got = passed_along(packed, "blk", offset)
            piece = (
                got[:, :width],
                got[:, width : 2 * width],
                got[:, 2 * width].astype(jnp.int32),
            )
            state = fold_block(state, piece)
    top, total, acc = state
    attn = (acc / total[..., None]).astype(jnp.bfloat16)
    attn = jnp.transpose(attn, (1, 0, 2)).reshape(rows, local_heads * HD)
    n_head = lax.axis_size("head")
    share = rows // n_head
    width = x_in.shape[1]
    full_proj_weight = lax.all_gather(proj_weight, "blk", axis=0, tiled=True)
    attn_part = jnp.dot(attn, out_weight, preferred_element_type=jnp.float32).astype(jnp.bfloat16)
    attn_pieces = lax.all_to_all(attn_part.reshape(n_head, share, width), "head", 0, 0, tiled=True)
    x_mine = lax.dynamic_slice_in_dim(x_in, lax.axis_index("head") * share, share, 0)
    h_one = x_mine + jnp.sum(attn_pieces.astype(jnp.float32), axis=0)
    n_two = gather_rows(layer_norm(h_one, ln2_gain, ln2_bias).astype(jnp.bfloat16), n_head)
    hidden = jax.nn.gelu(
        jnp.dot(n_two, fc1_weight, preferred_element_type=jnp.float32), approximate=False
    ).astype(jnp.bfloat16)
    mlp_part = jnp.dot(hidden, fc2_weight, preferred_element_type=jnp.float32).astype(jnp.bfloat16)
    pieces = lax.all_to_all(mlp_part.reshape(n_head, share, width), "head", 0, 0, tiled=True)
    layer_mine = (h_one + jnp.sum(pieces.astype(jnp.float32), axis=0)).astype(jnp.bfloat16)
    layer_mine, full_proj_weight = lax.optimization_barrier((layer_mine, full_proj_weight))
    layer = gather_rows(layer_mine, n_head)
    grouped = layer.reshape(rows // 4, 4 * layer.shape[1])
    proj = jnp.dot(
        grouped,
        full_proj_weight,
        preferred_element_type=jnp.float32,
    )
    requests = lax.axis_size("blk") // 2
    onehot = (group_segment[:, None] == jnp.arange(requests, dtype=jnp.int32)[None, :]).astype(
        jnp.float32
    )
    row_sq = jnp.sum(proj * proj, axis=1)
    local_sq = jnp.dot(row_sq, onehot, precision=lax.Precision.HIGHEST)
    local_count = jnp.sum(onehot, axis=0)
    row_top = jnp.max(jnp.abs(proj), axis=1)
    local_peak = jnp.max(jnp.where(onehot > 0.0, row_top[:, None], 0.0), axis=0)
    summed, req_peak = butterfly(jnp.concatenate([local_sq, local_count]), local_peak)
    tot_sq, tot_count = summed[:requests], summed[requests:]
    counts = tot_count / lax.axis_size("head")
    req_rms = jnp.sqrt(tot_sq / (counts * OUTW) + 1e-06)
    row_rms = jnp.dot(onehot, req_rms, precision=lax.Precision.HIGHEST)
    merged_out = (proj / row_rms[:, None]).astype(jnp.bfloat16)
    return (merged_out, req_rms, req_peak)


def solution(mesh):
    placed = (
        P("blk", None),
        P("blk"),
        P(),
        P(),
        P(None, None, "head"),
        P("head", None),
        P(),
        P(),
        P(None, "head"),
        P("head", None),
        P("blk", "head"),
    )
    return jax.shard_map(
        per_device,
        mesh=mesh,
        in_specs=placed,
        out_specs=(P("blk", "head"), P(), P()),
        check_vma=False,
    )
```

```python
import jax
import jax.numpy as jnp
from jax import lax
from jax.sharding import PartitionSpec as P

HD = 88
OUTW = 4096
REACH = 4


def passed_along(x, axis, by):
    size = lax.axis_size(axis)
    pairs = [(i, i + by) for i in range(size) if 0 <= i + by < size]
    return lax.ppermute(x, axis, pairs)


def butterfly(summed, peak):
    split = summed.shape[0]
    both = jnp.concatenate([summed, peak])
    for axis in ("head", "blk"):
        size = lax.axis_size(axis)
        if size & (size - 1):
            both = jnp.concatenate(
                [lax.psum(both[:split], axis), lax.pmax(both[split:], axis)]
            )
            continue
        step = 1
        while step < size:
            pairs = [(i, i ^ step) for i in range(size)]
            other = lax.ppermute(both, axis, pairs)
            both = jnp.concatenate(
                [both[:split] + other[:split], jnp.maximum(both[split:], other[split:])]
            )
            step *= 2
    return both[:split], both[split:]


def gather_rows(x, n_head):
    spread = jnp.broadcast_to(x[None], (n_head,) + x.shape)
    got = lax.all_to_all(spread, "head", 0, 0, tiled=True)
    return got.reshape((n_head * x.shape[0],) + x.shape[1:])


def layer_norm(x, gain, bias):
    mean = jnp.mean(x, axis=-1, keepdims=True)
    var = jnp.mean((x - mean) ** 2, axis=-1, keepdims=True)
    return (x - mean) * lax.rsqrt(var + 1e-06) * gain + bias


def per_device(
    tokens,
    group_segment,
    ln1_gain,
    ln1_bias,
    qkv_weight,
    out_weight,
    ln2_gain,
    ln2_bias,
    fc1_weight,
    fc2_weight,
    proj_weight,
):
    rows = tokens.shape[0]
    x_in = tokens.astype(jnp.float32)
    seg_ids = jnp.repeat(group_segment + 1, 4)
    own_low = jnp.min(seg_ids)
    own_high = jnp.max(seg_ids)
    normed = layer_norm(x_in, ln1_gain, ln1_bias).astype(jnp.bfloat16)
    qkv = jnp.einsum("rd,dck->crk", normed, qkv_weight, preferred_element_type=jnp.float32).astype(
        jnp.bfloat16
    )
    local_heads = qkv.shape[2] // HD
    query = qkv[0].reshape(rows, local_heads, HD)
    keys = qkv[1]
    values = qkv[2]
    scale = 1.0 / HD**0.5

    def update(carry, piece):
        top, total, acc = carry
        kpiece, vpiece, ipiece = piece
        count = kpiece.shape[0]
        scores = (
            jnp.einsum(
                "rhe,phe->hrp",
                query,
                kpiece.reshape(count, local_heads, HD),
                preferred_element_type=jnp.float32,
            )
            * scale
        )
        mask = (seg_ids[:, None] == ipiece[None, :])[None]
        new_top = jnp.maximum(top, jnp.max(jnp.where(mask, scores, -1e30), axis=-1))
        factor = jnp.exp(top - new_top)
        weights = jnp.where(mask, jnp.exp(scores - new_top[..., None]), 0.0)
        total = total * factor + jnp.sum(weights, axis=-1)
        acc = acc * factor[..., None] + jnp.einsum(
            "hrp,phe->hre",
            weights.astype(jnp.bfloat16),
            vpiece.reshape(count, local_heads, HD),
            preferred_element_type=jnp.float32,
        )
        return (new_top, total, acc)

    def fold_block(carry, piece):
        ipiece = piece[2]
        touches = (jnp.min(ipiece) <= own_high) & (jnp.max(ipiece) >= own_low)
        return lax.cond(touches, lambda c: update(c, piece), lambda c: c, carry)

    start_state = (
        jnp.full((local_heads, rows), -1e30, jnp.float32),
        jnp.zeros((local_heads, rows), jnp.float32),
        jnp.zeros((local_heads, rows, HD), jnp.float32),
    )
    state = fold_block(start_state, (keys, values, seg_ids))
    width = keys.shape[1]
    packed = jnp.concatenate(
        [keys, values, seg_ids.astype(jnp.bfloat16)[:, None]], axis=1
    )
    packed = jnp.pad(packed, ((0, 0), (0, (-packed.shape[1]) % 128)))
    for distance in range(1, REACH + 1):
        for offset in (distance, -distance):
            got = passed_along(packed, "blk", offset)
            piece = (
                got[:, :width],
                got[:, width : 2 * width],
                got[:, 2 * width].astype(jnp.int32),
            )
            state = fold_block(state, piece)
    top, total, acc = state
    attn = (acc / total[..., None]).astype(jnp.bfloat16)
    attn = jnp.transpose(attn, (1, 0, 2)).reshape(rows, local_heads * HD)
    n_head = lax.axis_size("head")
    share = rows // n_head
    width = x_in.shape[1]
    half = proj_weight.shape[1] // 2
    full_proj_weight = [
        lax.all_gather(proj_weight[:, :half], "blk", axis=0, tiled=True),
        lax.all_gather(proj_weight[:, half:], "blk", axis=0, tiled=True),
    ]
    attn_part = jnp.dot(attn, out_weight, preferred_element_type=jnp.float32).astype(jnp.bfloat16)
    attn_pieces = lax.all_to_all(attn_part.reshape(n_head, share, width), "head", 0, 0, tiled=True)
    x_mine = lax.dynamic_slice_in_dim(x_in, lax.axis_index("head") * share, share, 0)
    h_one = x_mine + jnp.sum(attn_pieces.astype(jnp.float32), axis=0)
    n_two = gather_rows(layer_norm(h_one, ln2_gain, ln2_bias).astype(jnp.bfloat16), n_head)
    hidden = jax.nn.gelu(
        jnp.dot(n_two, fc1_weight, preferred_element_type=jnp.float32), approximate=False
    ).astype(jnp.bfloat16)
    mlp_part = jnp.dot(hidden, fc2_weight, preferred_element_type=jnp.float32).astype(jnp.bfloat16)
    pieces = lax.all_to_all(mlp_part.reshape(n_head, share, width), "head", 0, 0, tiled=True)
    layer_mine = (h_one + jnp.sum(pieces.astype(jnp.float32), axis=0)).astype(jnp.bfloat16)
    layer_mine, full_proj_weight = lax.optimization_barrier((layer_mine, full_proj_weight))
    layer = gather_rows(layer_mine, n_head)
    grouped = layer.reshape(rows // 4, 4 * layer.shape[1])
    proj = jnp.dot(
        grouped,
        jnp.concatenate(full_proj_weight, axis=1),
        preferred_element_type=jnp.float32,
    )
    requests = lax.axis_size("blk") // 2
    onehot = (group_segment[:, None] == jnp.arange(requests, dtype=jnp.int32)[None, :]).astype(
        jnp.float32
    )
    row_sq = jnp.sum(proj * proj, axis=1)
    local_sq = jnp.dot(row_sq, onehot, precision=lax.Precision.HIGHEST)
    local_count = jnp.sum(onehot, axis=0)
    row_top = jnp.max(jnp.abs(proj), axis=1)
    local_peak = jnp.max(jnp.where(onehot > 0.0, row_top[:, None], 0.0), axis=0)
    summed, req_peak = butterfly(jnp.concatenate([local_sq, local_count]), local_peak)
    tot_sq, tot_count = summed[:requests], summed[requests:]
    counts = tot_count / lax.axis_size("head")
    req_rms = jnp.sqrt(tot_sq / (counts * OUTW) + 1e-06)
    row_rms = jnp.dot(onehot, req_rms, precision=lax.Precision.HIGHEST)
    merged_out = (proj / row_rms[:, None]).astype(jnp.bfloat16)
    return (merged_out, req_rms, req_peak)


def solution(mesh):
    placed = (
        P("blk", None),
        P("blk"),
        P(),
        P(),
        P(None, None, "head"),
        P("head", None),
        P(),
        P(),
        P(None, "head"),
        P("head", None),
        P("blk", "head"),
    )
    return jax.shard_map(
        per_device,
        mesh=mesh,
        in_specs=placed,
        out_specs=(P("blk", "head"), P(), P()),
        check_vma=False,
    )
```

```python
import jax
import jax.numpy as jnp
from jax import lax
from jax.sharding import PartitionSpec as P

HD = 88
OUTW = 4096
REACH = 4


def passed_along(x, axis, by):
    size = lax.axis_size(axis)
    pairs = [(i, i + by) for i in range(size) if 0 <= i + by < size]
    return lax.ppermute(x, axis, pairs)


def butterfly(summed, peak):
    split = summed.shape[0]
    both = jnp.concatenate([summed, peak])
    for axis in ("head", "blk"):
        size = lax.axis_size(axis)
        if size & (size - 1):
            both = jnp.concatenate(
                [lax.psum(both[:split], axis), lax.pmax(both[split:], axis)]
            )
            continue
        step = 1
        while step < size:
            pairs = [(i, i ^ step) for i in range(size)]
            other = lax.ppermute(both, axis, pairs)
            both = jnp.concatenate(
                [both[:split] + other[:split], jnp.maximum(both[split:], other[split:])]
            )
            step *= 2
    return both[:split], both[split:]


def gather_rows(x, n_head):
    spread = jnp.broadcast_to(x[None], (n_head,) + x.shape)
    got = lax.all_to_all(spread, "head", 0, 0, tiled=True)
    return got.reshape((n_head * x.shape[0],) + x.shape[1:])


def layer_norm(x, gain, bias):
    mean = jnp.mean(x, axis=-1, keepdims=True)
    var = jnp.mean((x - mean) ** 2, axis=-1, keepdims=True)
    return (x - mean) * lax.rsqrt(var + 1e-06) * gain + bias


def per_device(
    tokens,
    group_segment,
    ln1_gain,
    ln1_bias,
    qkv_weight,
    out_weight,
    ln2_gain,
    ln2_bias,
    fc1_weight,
    fc2_weight,
    proj_weight,
):
    rows = tokens.shape[0]
    x_in = tokens.astype(jnp.float32)
    seg_ids = jnp.repeat(group_segment + 1, 4)
    normed = layer_norm(x_in, ln1_gain, ln1_bias).astype(jnp.bfloat16)
    qkv = jnp.einsum("rd,dck->crk", normed, qkv_weight, preferred_element_type=jnp.float32).astype(
        jnp.bfloat16
    )
    local_heads = qkv.shape[2] // HD
    query = qkv[0].reshape(rows, local_heads, HD)
    keys = qkv[1]
    values = qkv[2]
    scale = 1.0 / HD**0.5

    width = keys.shape[1]
    packed = jnp.concatenate(
        [keys, values, seg_ids.astype(jnp.bfloat16)[:, None]], axis=1
    )
    packed = jnp.pad(packed, ((0, 0), (0, (-packed.shape[1]) % 128)))
    blocks = [packed]
    for distance in range(1, REACH + 1):
        for offset in (distance, -distance):
            blocks.append(passed_along(packed, "blk", offset))
    near = jnp.concatenate(blocks, axis=0)
    count = near.shape[0]
    near_keys = near[:, :width].reshape(count, local_heads, HD)
    near_values = near[:, width : 2 * width].reshape(count, local_heads, HD)
    near_seg = near[:, 2 * width].astype(jnp.int32)
    mask = (seg_ids[:, None] == near_seg[None, :])[None]
    scores = (
        jnp.einsum("rhe,phe->hrp", query, near_keys, preferred_element_type=jnp.float32)
        * scale
    )
    top = jnp.max(jnp.where(mask, scores, -1e30), axis=-1)
    weights = jnp.where(mask, jnp.exp(scores - top[..., None]), 0.0)
    total = jnp.sum(weights, axis=-1)
    acc = jnp.einsum(
        "hrp,phe->hre",
        weights.astype(jnp.bfloat16),
        near_values,
        preferred_element_type=jnp.float32,
    )
    attn = (acc / total[..., None]).astype(jnp.bfloat16)
    attn = jnp.transpose(attn, (1, 0, 2)).reshape(rows, local_heads * HD)
    n_head = lax.axis_size("head")
    share = rows // n_head
    width = x_in.shape[1]
    full_proj_weight = lax.all_gather(proj_weight, "blk", axis=0, tiled=True)
    attn_part = jnp.dot(attn, out_weight, preferred_element_type=jnp.float32).astype(jnp.bfloat16)
    attn_pieces = lax.all_to_all(attn_part.reshape(n_head, share, width), "head", 0, 0, tiled=True)
    x_mine = lax.dynamic_slice_in_dim(x_in, lax.axis_index("head") * share, share, 0)
    h_one = x_mine + jnp.sum(attn_pieces.astype(jnp.float32), axis=0)
    n_two = gather_rows(layer_norm(h_one, ln2_gain, ln2_bias).astype(jnp.bfloat16), n_head)
    hidden = jax.nn.gelu(
        jnp.dot(n_two, fc1_weight, preferred_element_type=jnp.float32), approximate=False
    ).astype(jnp.bfloat16)
    mlp_part = jnp.dot(hidden, fc2_weight, preferred_element_type=jnp.float32).astype(jnp.bfloat16)
    pieces = lax.all_to_all(mlp_part.reshape(n_head, share, width), "head", 0, 0, tiled=True)
    layer_mine = (h_one + jnp.sum(pieces.astype(jnp.float32), axis=0)).astype(jnp.bfloat16)
    layer_mine, full_proj_weight = lax.optimization_barrier((layer_mine, full_proj_weight))
    layer = gather_rows(layer_mine, n_head)
    grouped = layer.reshape(rows // 4, 4 * layer.shape[1])
    proj = jnp.dot(
        grouped,
        full_proj_weight,
        preferred_element_type=jnp.float32,
    )
    requests = lax.axis_size("blk") // 2
    onehot = (group_segment[:, None] == jnp.arange(requests, dtype=jnp.int32)[None, :]).astype(
        jnp.float32
    )
    row_sq = jnp.sum(proj * proj, axis=1)
    local_sq = jnp.dot(row_sq, onehot, precision=lax.Precision.HIGHEST)
    local_count = jnp.sum(onehot, axis=0)
    row_top = jnp.max(jnp.abs(proj), axis=1)
    local_peak = jnp.max(jnp.where(onehot > 0.0, row_top[:, None], 0.0), axis=0)
    summed, req_peak = butterfly(jnp.concatenate([local_sq, local_count]), local_peak)
    tot_sq, tot_count = summed[:requests], summed[requests:]
    counts = tot_count / lax.axis_size("head")
    req_rms = jnp.sqrt(tot_sq / (counts * OUTW) + 1e-06)
    row_rms = jnp.dot(onehot, req_rms, precision=lax.Precision.HIGHEST)
    merged_out = (proj / row_rms[:, None]).astype(jnp.bfloat16)
    return (merged_out, req_rms, req_peak)


def solution(mesh):
    placed = (
        P("blk", None),
        P("blk"),
        P(),
        P(),
        P(None, None, "head"),
        P("head", None),
        P(),
        P(),
        P(None, "head"),
        P("head", None),
        P("blk", "head"),
    )
    return jax.shard_map(
        per_device,
        mesh=mesh,
        in_specs=placed,
        out_specs=(P("blk", "head"), P(), P()),
        check_vma=False,
    )
```

```python
import jax
import jax.numpy as jnp
from jax import lax
from jax.sharding import PartitionSpec as P

HD = 88
OUTW = 4096
REACH = 4


def passed_along(x, axis, by):
    size = lax.axis_size(axis)
    pairs = [(i, i + by) for i in range(size) if 0 <= i + by < size]
    return lax.ppermute(x, axis, pairs)


def butterfly(summed, peak):
    split = summed.shape[0]
    both = jnp.concatenate([summed, peak])
    for axis in ("head", "blk"):
        size = lax.axis_size(axis)
        if size & (size - 1):
            both = jnp.concatenate(
                [lax.psum(both[:split], axis), lax.pmax(both[split:], axis)]
            )
            continue
        step = 1
        while step < size:
            pairs = [(i, i ^ step) for i in range(size)]
            other = lax.ppermute(both, axis, pairs)
            both = jnp.concatenate(
                [both[:split] + other[:split], jnp.maximum(both[split:], other[split:])]
            )
            step *= 2
    return both[:split], both[split:]


def gather_rows(x, n_head):
    spread = jnp.broadcast_to(x[None], (n_head,) + x.shape)
    got = lax.all_to_all(spread, "head", 0, 0, tiled=True)
    return got.reshape((n_head * x.shape[0],) + x.shape[1:])


def layer_norm(x, gain, bias):
    mean = jnp.mean(x, axis=-1, keepdims=True)
    var = jnp.mean((x - mean) ** 2, axis=-1, keepdims=True)
    return (x - mean) * lax.rsqrt(var + 1e-06) * gain + bias


def per_device(
    tokens,
    group_segment,
    ln1_gain,
    ln1_bias,
    qkv_weight,
    out_weight,
    ln2_gain,
    ln2_bias,
    fc1_weight,
    fc2_weight,
    proj_weight,
):
    rows = tokens.shape[0]
    x_in = tokens.astype(jnp.float32)
    seg_ids = jnp.repeat(group_segment + 1, 4)
    normed = layer_norm(x_in, ln1_gain, ln1_bias).astype(jnp.bfloat16)
    qkv = jnp.einsum("rd,dck->crk", normed, qkv_weight, preferred_element_type=jnp.float32).astype(
        jnp.bfloat16
    )
    local_heads = qkv.shape[2] // HD
    query = qkv[0].reshape(rows, local_heads, HD)
    keys = qkv[1]
    values = qkv[2]
    scale = 1.0 / HD**0.5

    width = keys.shape[1]
    packed = jnp.concatenate(
        [keys, values, seg_ids.astype(jnp.bfloat16)[:, None]], axis=1
    )
    packed = jnp.pad(packed, ((0, 0), (0, (-packed.shape[1]) % 128)))
    blocks = [packed]
    for distance in range(1, REACH + 1):
        for offset in (distance, -distance):
            blocks.append(passed_along(packed, "blk", offset))
    near = jnp.concatenate(blocks, axis=0)
    count = near.shape[0]
    near_keys = near[:, :width].reshape(count, local_heads, HD)
    near_values = near[:, width : 2 * width].reshape(count, local_heads, HD)
    near_seg = near[:, 2 * width].astype(jnp.int32)
    mask = (seg_ids[:, None] == near_seg[None, :])[None]
    scores = (
        jnp.einsum("rhe,phe->hrp", query, near_keys, preferred_element_type=jnp.float32)
        * scale
    )
    top = jnp.max(jnp.where(mask, scores, -1e30), axis=-1)
    weights = jnp.where(mask, jnp.exp(scores - top[..., None]), 0.0)
    total = jnp.sum(weights, axis=-1)
    acc = jnp.einsum(
        "hrp,phe->hre",
        weights.astype(jnp.bfloat16),
        near_values,
        preferred_element_type=jnp.float32,
    )
    attn = (acc / total[..., None]).astype(jnp.bfloat16)
    attn = jnp.transpose(attn, (1, 0, 2)).reshape(rows, local_heads * HD)
    n_head = lax.axis_size("head")
    share = rows // n_head
    width = x_in.shape[1]
    full_proj_weight = lax.all_gather(proj_weight, "blk", axis=0, tiled=True)
    attn_part = jnp.dot(attn, out_weight, preferred_element_type=jnp.float32).astype(jnp.bfloat16)
    attn_pieces = lax.all_to_all(attn_part.reshape(n_head, share, width), "head", 0, 0, tiled=True)
    x_mine = lax.dynamic_slice_in_dim(x_in, lax.axis_index("head") * share, share, 0)
    h_one = x_mine + jnp.sum(attn_pieces.astype(jnp.float32), axis=0)
    h_one, full_proj_weight = lax.optimization_barrier((h_one, full_proj_weight))
    n_two = gather_rows(layer_norm(h_one, ln2_gain, ln2_bias).astype(jnp.bfloat16), n_head)
    hidden = jax.nn.gelu(
        jnp.dot(n_two, fc1_weight, preferred_element_type=jnp.float32), approximate=False
    ).astype(jnp.bfloat16)
    mlp_part = jnp.dot(hidden, fc2_weight, preferred_element_type=jnp.float32).astype(jnp.bfloat16)
    pieces = lax.all_to_all(mlp_part.reshape(n_head, share, width), "head", 0, 0, tiled=True)
    layer_mine = (h_one + jnp.sum(pieces.astype(jnp.float32), axis=0)).astype(jnp.bfloat16)
    layer = gather_rows(layer_mine, n_head)
    grouped = layer.reshape(rows // 4, 4 * layer.shape[1])
    proj = jnp.dot(
        grouped,
        full_proj_weight,
        preferred_element_type=jnp.float32,
    )
    requests = lax.axis_size("blk") // 2
    onehot = (group_segment[:, None] == jnp.arange(requests, dtype=jnp.int32)[None, :]).astype(
        jnp.float32
    )
    row_sq = jnp.sum(proj * proj, axis=1)
    local_sq = jnp.dot(row_sq, onehot, precision=lax.Precision.HIGHEST)
    local_count = jnp.sum(onehot, axis=0)
    row_top = jnp.max(jnp.abs(proj), axis=1)
    local_peak = jnp.max(jnp.where(onehot > 0.0, row_top[:, None], 0.0), axis=0)
    summed, req_peak = butterfly(jnp.concatenate([local_sq, local_count]), local_peak)
    tot_sq, tot_count = summed[:requests], summed[requests:]
    counts = tot_count / lax.axis_size("head")
    req_rms = jnp.sqrt(tot_sq / (counts * OUTW) + 1e-06)
    row_rms = jnp.dot(onehot, req_rms, precision=lax.Precision.HIGHEST)
    merged_out = (proj / row_rms[:, None]).astype(jnp.bfloat16)
    return (merged_out, req_rms, req_peak)


def solution(mesh):
    placed = (
        P("blk", None),
        P("blk"),
        P(),
        P(),
        P(None, None, "head"),
        P("head", None),
        P(),
        P(),
        P(None, "head"),
        P("head", None),
        P("blk", "head"),
    )
    return jax.shard_map(
        per_device,
        mesh=mesh,
        in_specs=placed,
        out_specs=(P("blk", "head"), P(), P()),
        check_vma=False,
    )
```

```python
import jax
import jax.numpy as jnp
from jax import lax
from jax.sharding import PartitionSpec as P

HD = 88
OUTW = 4096
REACH = 4


def passed_along(x, axis, by):
    size = lax.axis_size(axis)
    pairs = [(i, i + by) for i in range(size) if 0 <= i + by < size]
    return lax.ppermute(x, axis, pairs)


def butterfly(summed, peak):
    split = summed.shape[0]
    both = jnp.concatenate([summed, peak])
    for axis in ("head", "blk"):
        size = lax.axis_size(axis)
        if size & (size - 1):
            both = jnp.concatenate(
                [lax.psum(both[:split], axis), lax.pmax(both[split:], axis)]
            )
            continue
        step = 1
        while step < size:
            pairs = [(i, i ^ step) for i in range(size)]
            other = lax.ppermute(both, axis, pairs)
            both = jnp.concatenate(
                [both[:split] + other[:split], jnp.maximum(both[split:], other[split:])]
            )
            step *= 2
    return both[:split], both[split:]


def gather_rows(x, n_head):
    spread = jnp.broadcast_to(x[None], (n_head,) + x.shape)
    got = lax.all_to_all(spread, "head", 0, 0, tiled=True)
    return got.reshape((n_head * x.shape[0],) + x.shape[1:])


def layer_norm(x, gain, bias):
    mean = jnp.mean(x, axis=-1, keepdims=True)
    var = jnp.mean((x - mean) ** 2, axis=-1, keepdims=True)
    return (x - mean) * lax.rsqrt(var + 1e-06) * gain + bias


def per_device(
    tokens,
    group_segment,
    ln1_gain,
    ln1_bias,
    qkv_weight,
    out_weight,
    ln2_gain,
    ln2_bias,
    fc1_weight,
    fc2_weight,
    proj_weight,
):
    rows = tokens.shape[0]
    x_in = tokens.astype(jnp.float32)
    seg_ids = jnp.repeat(group_segment + 1, 4)
    normed = layer_norm(x_in, ln1_gain, ln1_bias).astype(jnp.bfloat16)
    qkv = jnp.einsum("rd,dck->crk", normed, qkv_weight, preferred_element_type=jnp.float32).astype(
        jnp.bfloat16
    )
    local_heads = qkv.shape[2] // HD
    query = qkv[0].reshape(rows, local_heads, HD)
    keys = qkv[1]
    values = qkv[2]
    scale = 1.0 / HD**0.5

    width = keys.shape[1]
    packed = jnp.concatenate(
        [keys, values, seg_ids.astype(jnp.bfloat16)[:, None]], axis=1
    )
    blocks = [packed]
    for distance in range(1, REACH + 1):
        for offset in (distance, -distance):
            blocks.append(passed_along(packed, "blk", offset))
    near = jnp.concatenate(blocks, axis=0)
    count = near.shape[0]
    near_keys = near[:, :width].reshape(count, local_heads, HD)
    near_values = near[:, width : 2 * width].reshape(count, local_heads, HD)
    near_seg = near[:, 2 * width].astype(jnp.int32)
    mask = (seg_ids[:, None] == near_seg[None, :])[None]
    scores = (
        jnp.einsum("rhe,phe->hrp", query, near_keys, preferred_element_type=jnp.float32)
        * scale
    )
    top = jnp.max(jnp.where(mask, scores, -1e30), axis=-1)
    weights = jnp.where(mask, jnp.exp(scores - top[..., None]), 0.0)
    total = jnp.sum(weights, axis=-1)
    acc = jnp.einsum(
        "hrp,phe->hre",
        weights.astype(jnp.bfloat16),
        near_values,
        preferred_element_type=jnp.float32,
    )
    attn = (acc / total[..., None]).astype(jnp.bfloat16)
    attn = jnp.transpose(attn, (1, 0, 2)).reshape(rows, local_heads * HD)
    n_head = lax.axis_size("head")
    share = rows // n_head
    width = x_in.shape[1]
    full_proj_weight = lax.all_gather(proj_weight, "blk", axis=0, tiled=True)
    attn_part = jnp.dot(attn, out_weight, preferred_element_type=jnp.float32).astype(jnp.bfloat16)
    attn_pieces = lax.all_to_all(attn_part.reshape(n_head, share, width), "head", 0, 0, tiled=True)
    x_mine = lax.dynamic_slice_in_dim(x_in, lax.axis_index("head") * share, share, 0)
    h_one = x_mine + jnp.sum(attn_pieces.astype(jnp.float32), axis=0)
    h_one, full_proj_weight = lax.optimization_barrier((h_one, full_proj_weight))
    n_two = gather_rows(layer_norm(h_one, ln2_gain, ln2_bias).astype(jnp.bfloat16), n_head)
    hidden = jax.nn.gelu(
        jnp.dot(n_two, fc1_weight, preferred_element_type=jnp.float32), approximate=False
    ).astype(jnp.bfloat16)
    mlp_part = jnp.dot(hidden, fc2_weight, preferred_element_type=jnp.float32).astype(jnp.bfloat16)
    pieces = lax.all_to_all(mlp_part.reshape(n_head, share, width), "head", 0, 0, tiled=True)
    layer_mine = (h_one + jnp.sum(pieces.astype(jnp.float32), axis=0)).astype(jnp.bfloat16)
    layer = gather_rows(layer_mine, n_head)
    grouped = layer.reshape(rows // 4, 4 * layer.shape[1])
    proj = jnp.dot(
        grouped,
        full_proj_weight,
        preferred_element_type=jnp.float32,
    )
    requests = lax.axis_size("blk") // 2
    onehot = (group_segment[:, None] == jnp.arange(requests, dtype=jnp.int32)[None, :]).astype(
        jnp.float32
    )
    row_sq = jnp.sum(proj * proj, axis=1)
    local_sq = jnp.dot(row_sq, onehot, precision=lax.Precision.HIGHEST)
    local_count = jnp.sum(onehot, axis=0)
    row_top = jnp.max(jnp.abs(proj), axis=1)
    local_peak = jnp.max(jnp.where(onehot > 0.0, row_top[:, None], 0.0), axis=0)
    summed, req_peak = butterfly(jnp.concatenate([local_sq, local_count]), local_peak)
    tot_sq, tot_count = summed[:requests], summed[requests:]
    counts = tot_count / lax.axis_size("head")
    req_rms = jnp.sqrt(tot_sq / (counts * OUTW) + 1e-06)
    row_rms = jnp.dot(onehot, req_rms, precision=lax.Precision.HIGHEST)
    merged_out = (proj / row_rms[:, None]).astype(jnp.bfloat16)
    return (merged_out, req_rms, req_peak)


def solution(mesh):
    placed = (
        P("blk", None),
        P("blk"),
        P(),
        P(),
        P(None, None, "head"),
        P("head", None),
        P(),
        P(),
        P(None, "head"),
        P("head", None),
        P("blk", "head"),
    )
    return jax.shard_map(
        per_device,
        mesh=mesh,
        in_specs=placed,
        out_specs=(P("blk", "head"), P(), P()),
        check_vma=False,
    )
```

```python
import jax
import jax.numpy as jnp
from jax import lax
from jax.sharding import PartitionSpec as P

HD = 88
OUTW = 4096
REACH = 4


def passed_along(x, axis, by):
    size = lax.axis_size(axis)
    pairs = [(i, i + by) for i in range(size) if 0 <= i + by < size]
    return lax.ppermute(x, axis, pairs)


def butterfly(summed, peak):
    split = summed.shape[0]
    both = jnp.concatenate([summed, peak])
    for axis in ("head", "blk"):
        size = lax.axis_size(axis)
        if size & (size - 1):
            both = jnp.concatenate(
                [lax.psum(both[:split], axis), lax.pmax(both[split:], axis)]
            )
            continue
        step = 1
        while step < size:
            pairs = [(i, i ^ step) for i in range(size)]
            other = lax.ppermute(both, axis, pairs)
            both = jnp.concatenate(
                [both[:split] + other[:split], jnp.maximum(both[split:], other[split:])]
            )
            step *= 2
    return both[:split], both[split:]


def gather_rows(x, n_head):
    spread = jnp.broadcast_to(x[None], (n_head,) + x.shape)
    got = lax.all_to_all(spread, "head", 0, 0, tiled=True)
    return got.reshape((n_head * x.shape[0],) + x.shape[1:])


def layer_norm(x, gain, bias):
    mean = jnp.mean(x, axis=-1, keepdims=True)
    var = jnp.mean((x - mean) ** 2, axis=-1, keepdims=True)
    return (x - mean) * lax.rsqrt(var + 1e-06) * gain + bias


def per_device(
    tokens,
    group_segment,
    ln1_gain,
    ln1_bias,
    qkv_weight,
    out_weight,
    ln2_gain,
    ln2_bias,
    fc1_weight,
    fc2_weight,
    proj_weight,
):
    rows = tokens.shape[0]
    x_in = tokens.astype(jnp.float32)
    seg_ids = jnp.repeat(group_segment + 1, 4)
    normed = layer_norm(x_in, ln1_gain, ln1_bias).astype(jnp.bfloat16)
    qkv = jnp.einsum("rd,dck->crk", normed, qkv_weight, preferred_element_type=jnp.float32).astype(
        jnp.bfloat16
    )
    local_heads = qkv.shape[2] // HD
    query = qkv[0].reshape(rows, local_heads, HD)
    keys = qkv[1]
    values = qkv[2]
    scale = 1.0 / HD**0.5

    width = keys.shape[1]
    packed = jnp.concatenate(
        [keys, values, seg_ids.astype(jnp.bfloat16)[:, None]], axis=1
    )
    blocks = [packed]
    for distance in range(1, REACH + 1):
        for offset in (distance, -distance):
            blocks.append(passed_along(packed, "blk", offset))
    near = jnp.concatenate(blocks, axis=0)
    count = near.shape[0]
    near_keys = near[:, :width].reshape(count, local_heads, HD)
    near_values = near[:, width : 2 * width].reshape(count, local_heads, HD)
    near_seg = near[:, 2 * width].astype(jnp.int32)
    mask = (seg_ids[:, None] == near_seg[None, :])[None]
    scores = (
        jnp.einsum("rhe,phe->hrp", query, near_keys, preferred_element_type=jnp.float32)
        * scale
    )
    top = jnp.max(jnp.where(mask, scores, -1e30), axis=-1)
    weights = jnp.where(mask, jnp.exp(scores - top[..., None]), 0.0)
    total = jnp.sum(weights, axis=-1)
    acc = jnp.einsum(
        "hrp,phe->hre",
        weights.astype(jnp.bfloat16),
        near_values,
        preferred_element_type=jnp.float32,
    )
    attn = (acc / total[..., None]).astype(jnp.bfloat16)
    attn = jnp.transpose(attn, (1, 0, 2)).reshape(rows, local_heads * HD)
    n_head = lax.axis_size("head")
    share = rows // n_head
    width = x_in.shape[1]
    full_proj_weight = lax.all_gather(proj_weight, "blk", axis=0, tiled=True)
    attn_part = jnp.dot(attn, out_weight, preferred_element_type=jnp.float32).astype(jnp.bfloat16)
    attn_pieces = lax.all_to_all(attn_part.reshape(n_head, share, width), "head", 0, 0, tiled=True)
    x_mine = lax.dynamic_slice_in_dim(x_in, lax.axis_index("head") * share, share, 0)
    h_one = x_mine + jnp.sum(attn_pieces.astype(jnp.float32), axis=0)
    n_two = gather_rows(layer_norm(h_one, ln2_gain, ln2_bias).astype(jnp.bfloat16), n_head)
    hidden = jax.nn.gelu(
        jnp.dot(n_two, fc1_weight, preferred_element_type=jnp.float32), approximate=False
    ).astype(jnp.bfloat16)
    mlp_part = jnp.dot(hidden, fc2_weight, preferred_element_type=jnp.float32).astype(jnp.bfloat16)
    mlp_part, full_proj_weight = lax.optimization_barrier((mlp_part, full_proj_weight))
    pieces = lax.all_to_all(mlp_part.reshape(n_head, share, width), "head", 0, 0, tiled=True)
    layer_mine = (h_one + jnp.sum(pieces.astype(jnp.float32), axis=0)).astype(jnp.bfloat16)
    layer = gather_rows(layer_mine, n_head)
    grouped = layer.reshape(rows // 4, 4 * layer.shape[1])
    proj = jnp.dot(
        grouped,
        full_proj_weight,
        preferred_element_type=jnp.float32,
    )
    requests = lax.axis_size("blk") // 2
    onehot = (group_segment[:, None] == jnp.arange(requests, dtype=jnp.int32)[None, :]).astype(
        jnp.float32
    )
    row_sq = jnp.sum(proj * proj, axis=1)
    local_sq = jnp.dot(row_sq, onehot, precision=lax.Precision.HIGHEST)
    local_count = jnp.sum(onehot, axis=0)
    row_top = jnp.max(jnp.abs(proj), axis=1)
    local_peak = jnp.max(jnp.where(onehot > 0.0, row_top[:, None], 0.0), axis=0)
    summed, req_peak = butterfly(jnp.concatenate([local_sq, local_count]), local_peak)
    tot_sq, tot_count = summed[:requests], summed[requests:]
    counts = tot_count / lax.axis_size("head")
    req_rms = jnp.sqrt(tot_sq / (counts * OUTW) + 1e-06)
    row_rms = jnp.dot(onehot, req_rms, precision=lax.Precision.HIGHEST)
    merged_out = (proj / row_rms[:, None]).astype(jnp.bfloat16)
    return (merged_out, req_rms, req_peak)


def solution(mesh):
    placed = (
        P("blk", None),
        P("blk"),
        P(),
        P(),
        P(None, None, "head"),
        P("head", None),
        P(),
        P(),
        P(None, "head"),
        P("head", None),
        P("blk", "head"),
    )
    return jax.shard_map(
        per_device,
        mesh=mesh,
        in_specs=placed,
        out_specs=(P("blk", "head"), P(), P()),
        check_vma=False,
    )
```

```python
import jax
import jax.numpy as jnp
from jax import lax
from jax.sharding import PartitionSpec as P

HD = 88
OUTW = 4096
REACH = 4


def passed_along(x, axis, by):
    size = lax.axis_size(axis)
    pairs = [(i, i + by) for i in range(size) if 0 <= i + by < size]
    return lax.ppermute(x, axis, pairs)


def butterfly(summed, peak):
    split = summed.shape[0]
    both = jnp.concatenate([summed, peak])
    for axis in ("head", "blk"):
        size = lax.axis_size(axis)
        if size & (size - 1):
            both = jnp.concatenate(
                [lax.psum(both[:split], axis), lax.pmax(both[split:], axis)]
            )
            continue
        step = 1
        while step < size:
            pairs = [(i, i ^ step) for i in range(size)]
            other = lax.ppermute(both, axis, pairs)
            both = jnp.concatenate(
                [both[:split] + other[:split], jnp.maximum(both[split:], other[split:])]
            )
            step *= 2
    return both[:split], both[split:]


def gather_rows(x, n_head):
    spread = jnp.broadcast_to(x[None], (n_head,) + x.shape)
    got = lax.all_to_all(spread, "head", 0, 0, tiled=True)
    return got.reshape((n_head * x.shape[0],) + x.shape[1:])


def layer_norm(x, gain, bias):
    mean = jnp.mean(x, axis=-1, keepdims=True)
    var = jnp.mean((x - mean) ** 2, axis=-1, keepdims=True)
    return (x - mean) * lax.rsqrt(var + 1e-06) * gain + bias


def per_device(
    tokens,
    group_segment,
    ln1_gain,
    ln1_bias,
    qkv_weight,
    out_weight,
    ln2_gain,
    ln2_bias,
    fc1_weight,
    fc2_weight,
    proj_weight,
):
    rows = tokens.shape[0]
    x_in = tokens.astype(jnp.float32)
    seg_ids = jnp.repeat(group_segment + 1, 4)
    normed = layer_norm(x_in, ln1_gain, ln1_bias).astype(jnp.bfloat16)
    qkv = jnp.einsum("rd,dck->crk", normed, qkv_weight, preferred_element_type=jnp.float32).astype(
        jnp.bfloat16
    )
    local_heads = qkv.shape[2] // HD
    query = qkv[0].reshape(rows, local_heads, HD)
    keys = qkv[1]
    values = qkv[2]
    scale = 1.0 / HD**0.5

    width = keys.shape[1]
    packed = jnp.concatenate(
        [keys, values, seg_ids.astype(jnp.bfloat16)[:, None]], axis=1
    )
    blocks = [packed]
    for distance in range(1, REACH + 1):
        for offset in (distance, -distance):
            blocks.append(passed_along(packed, "blk", offset))
    near = jnp.concatenate(blocks, axis=0)
    count = near.shape[0]
    near_keys = near[:, :width].reshape(count, local_heads, HD)
    near_values = near[:, width : 2 * width].reshape(count, local_heads, HD)
    near_seg = near[:, 2 * width].astype(jnp.int32)
    mask = (seg_ids[:, None] == near_seg[None, :])[None]
    scores = (
        jnp.einsum("rhe,phe->hrp", query, near_keys, preferred_element_type=jnp.float32)
        * scale
    )
    top = jnp.max(jnp.where(mask, scores, -1e30), axis=-1)
    weights = jnp.where(mask, jnp.exp(scores - top[..., None]), 0.0)
    total = jnp.sum(weights, axis=-1)
    acc = jnp.einsum(
        "hrp,phe->hre",
        weights.astype(jnp.bfloat16),
        near_values,
        preferred_element_type=jnp.float32,
    )
    attn = (acc / total[..., None]).astype(jnp.bfloat16)
    attn = jnp.transpose(attn, (1, 0, 2)).reshape(rows, local_heads * HD)
    n_head = lax.axis_size("head")
    share = rows // n_head
    width = x_in.shape[1]
    full_proj_weight = lax.all_gather(proj_weight, "blk", axis=0, tiled=True)
    attn_part = jnp.dot(attn, out_weight, preferred_element_type=jnp.float32).astype(jnp.bfloat16)
    attn_pieces = lax.all_to_all(attn_part.reshape(n_head, share, width), "head", 0, 0, tiled=True)
    x_mine = lax.dynamic_slice_in_dim(x_in, lax.axis_index("head") * share, share, 0)
    h_one = x_mine + jnp.sum(attn_pieces.astype(jnp.float32), axis=0)
    h_one, full_proj_weight = lax.optimization_barrier((h_one, full_proj_weight))
    n_two = gather_rows(layer_norm(h_one, ln2_gain, ln2_bias).astype(jnp.bfloat16), n_head)
    hidden = jax.nn.gelu(
        jnp.dot(n_two, fc1_weight, preferred_element_type=jnp.float32), approximate=False
    ).astype(jnp.bfloat16)
    mlp_part = jnp.dot(hidden, fc2_weight, preferred_element_type=jnp.float32).astype(jnp.bfloat16)
    pieces = lax.all_to_all(mlp_part.reshape(n_head, share, width), "head", 0, 0, tiled=True)
    layer_mine = (h_one + jnp.sum(pieces.astype(jnp.float32), axis=0)).astype(jnp.bfloat16)
    grouped = gather_rows(layer_mine.reshape(share // 4, 4 * width), n_head)
    proj = jnp.dot(
        grouped,
        full_proj_weight,
        preferred_element_type=jnp.float32,
    )
    requests = lax.axis_size("blk") // 2
    onehot = (group_segment[:, None] == jnp.arange(requests, dtype=jnp.int32)[None, :]).astype(
        jnp.float32
    )
    row_sq = jnp.sum(proj * proj, axis=1)
    local_sq = jnp.dot(row_sq, onehot, precision=lax.Precision.HIGHEST)
    local_count = jnp.sum(onehot, axis=0)
    row_top = jnp.max(jnp.abs(proj), axis=1)
    local_peak = jnp.max(jnp.where(onehot > 0.0, row_top[:, None], 0.0), axis=0)
    summed, req_peak = butterfly(jnp.concatenate([local_sq, local_count]), local_peak)
    tot_sq, tot_count = summed[:requests], summed[requests:]
    counts = tot_count / lax.axis_size("head")
    req_rms = jnp.sqrt(tot_sq / (counts * OUTW) + 1e-06)
    row_rms = jnp.dot(onehot, req_rms, precision=lax.Precision.HIGHEST)
    merged_out = (proj / row_rms[:, None]).astype(jnp.bfloat16)
    return (merged_out, req_rms, req_peak)


def solution(mesh):
    placed = (
        P("blk", None),
        P("blk"),
        P(),
        P(),
        P(None, None, "head"),
        P("head", None),
        P(),
        P(),
        P(None, "head"),
        P("head", None),
        P("blk", "head"),
    )
    return jax.shard_map(
        per_device,
        mesh=mesh,
        in_specs=placed,
        out_specs=(P("blk", "head"), P(), P()),
        check_vma=False,
    )
```
